512 devices in a mesh: seq: 16 (over y, core), exp: 32 (over z, x).
Axes of the slice: x: 4, y: 8, z: 8, core: 2. Of those that a mesh axis runs over, the one named last changes fastest.
Arguments:
- x_act: bfloat16 [32, 2048, 4096], P('exp', 'seq'), may hold values from -6 to 6
- dt_low: bfloat16 [32, 2048, 256], P('exp', 'seq'), may hold values from -6 to 6
- b_c: float32 [32, 2048, 32], P('exp', 'seq'), may hold values from -6 to 6
- w_dt: bfloat16 [256, 4096], replicated, may hold values from -0.375 to 0.375
- dt_bias: float32 [4096], replicated, may hold values from -6 to -1
- a_log: float32 [16, 4096], replicated, may hold values from -1 to 2
- d_skip: float32 [4096], replicated, may hold values from 0.5 to 1.5
- w_router: bfloat16 [16, 4096], replicated, may hold values from -0.09375 to 0.09375
- expert_ids: int32 [32, 2048, 2], P('exp', 'seq'), may hold values from 0 to 15, all different within a row; in each aligned block of 128 rows (0 to 127, 128 to 255, ..., all dimensions but the last counted through in order) at most 20 rows name the same one
- w_up: bfloat16 [32, 4096, 640], P('exp', 'seq'), may hold values from -0.09375 to 0.09375
- w_down: bfloat16 [32, 640, 4096], P('exp', None, 'seq'), may hold values from -0.15625 to 0.15625
Outputs:
- layer_out: bfloat16 [32, 2048, 4096], P('exp', 'seq')
The draws below stay inside these ranges and needn't reach their ends.
Inputs may be any that keep to these rules, and one draw needn't show every extreme that they name: `expert_ids`: within the 128 tokens of one device (an aligned block), no expert is chosen by more than 20 tokens, and in some blocks one expert is chosen by exactly 20; a token's two experts differ.
All inputs are finite; a program needn't handle non-finite values.
Results may differ from the reference program's by a relative error of at most 0.011.
Values may be sent and summed in bfloat16 or wider, within the bound.
No kernel may reach another device: no remote copies, remote signals or barrier semaphores. Data moves between devices by JAX's collectives and lax.ppermute only.
A program may use at most 128 MiB of HBM per device.

```python
import math
import jax
import jax.numpy as jnp
import numpy as np
from jax import lax

WIDTH = 4096
RANK = 256
NS = 16
EH = 640
TOK = 128
RECORDS = 32
LENGTH = 2048
EXPERTS = 16
CAP = 20
N_EXP = 32


def block_levels(stream_key, extent, split, least, top_value):
    def one(dim, shards_of):
        steps = jax.random.uniform(jax.random.fold_in(jax.random.fold_in(stream_key, 6), dim), (shards_of,), jnp.float32, least / len(split), top_value / len(split))
        return jnp.repeat(jnp.exp(steps), extent[dim] // shards_of).reshape((-1,) + (1,) * (len(extent) - dim - 1))

    factor_of = one(*split[0])
    for cut in split[1:]:
        factor_of = factor_of * one(*cut)
    return factor_of


def deal_out(stream_key, own, number, rows, amount, top, bound, slope):
    sequence = jax.random.permutation(stream_key, amount)
    heavy_load, ordinary = load_shares(amount, rows * top, bound, slope, True), load_shares(amount, rows * top, bound, slope, False)
    places = jnp.arange(amount)

    def named(tallies, rotation):
        used = int((tallies > 0).sum())
        fixed = max(1, used // 4)
        passed = fixed + (places - fixed + rotation * (used - fixed)) % max(1, amount - fixed)
        return jnp.zeros((amount,), jnp.int32).at[sequence[jnp.where(places < fixed, places, passed)]].set(jnp.asarray(tallies, jnp.int32))

    tallies = jnp.where(number % 4 == 0, named(heavy_load, number // 4), named(ordinary, number - number // 4 - 1))
    mixed = jax.random.permutation(jax.random.fold_in(own, 3), amount)
    giver, receiver = mixed[0:amount // 2 * 2:2], mixed[1:amount // 2 * 2:2]
    room = jnp.minimum(tallies[giver] - 1, bound - tallies[receiver]) // 2
    room = jnp.where((giver == sequence[0]) | (receiver == sequence[0]) | (tallies[receiver] == 0), 0, jnp.maximum(room, 0))
    passed = jax.random.randint(jax.random.fold_in(own, 4), (amount // 2,), 0, 1 << 20) % (room + 1)
    tallies = tallies.at[giver].add(-passed).at[receiver].add(passed)
    labels = jnp.searchsorted(jnp.cumsum(tallies), jnp.arange(rows * top), side="right").astype(jnp.int32)
    grid = labels.reshape(top, rows).T
    grid = grid[jax.random.permutation(jax.random.fold_in(own, 1), rows)]
    rotation = jax.random.randint(jax.random.fold_in(own, 2), (rows, 1), 0, top)
    return jnp.take_along_axis(grid, (jnp.arange(top)[None, :] + rotation) % top, axis=1)


def load_shares(number_of, total, bound, skew, full):
    portions = [(1 << 20) // math.isqrt(grade ** skew) + 1 for grade in range(1, number_of + 1)]
    largest = bound if full else min(bound, max(-(-total // number_of), total * portions[0] // sum(portions)))
    least = 1 if total - largest >= number_of - 1 else 0
    counts, rest = [largest] + [least] * (number_of - 1), total - largest - least * (number_of - 1)
    while rest > 0:
        movable = [i for i in range(1, number_of) if counts[i] < largest] or [i for i in range(1, number_of) if counts[i] < bound]
        mass, budget = sum([portions[i] for i in movable]), rest
        for i in movable:
            more = min(bound - counts[i], max(1, budget * portions[i] // mass), rest)
            counts[i] = counts[i] + more
            rest = rest - more
    return np.array(counts)


def bell_draw(stream_key, dims, scale, bound, pieces=(), kind=jnp.bfloat16):
    gain = block_levels(stream_key, dims, pieces, -0.22, 0.18) if pieces else 1.0
    drawn = jax.random.normal(stream_key, dims, jnp.float32) * scale * gain
    return jnp.minimum(jnp.maximum(drawn, -bound), bound).astype(kind)


def setup_inputs(seed: int = 0) -> dict:
    key_of = jax.random.split(jax.random.key(seed), 12)
    x_act = bell_draw(key_of[0], (RECORDS, LENGTH, WIDTH), 1.0, 6.0, ((0, 32), (1, 16)))
    dt_low = bell_draw(key_of[1], (RECORDS, LENGTH, RANK), 1.0, 6.0, ((0, 32), (1, 16)))
    b_c = bell_draw(key_of[2], (RECORDS, LENGTH, 2 * NS), 1.0, 6.0, ((0, 32), (1, 16)), jnp.float32)
    w_dt = bell_draw(key_of[3], (RANK, WIDTH), RANK ** -0.5, 0.375)
    dt_bias = jnp.clip(jax.random.uniform(key_of[4], (WIDTH,), jnp.float32, -6.0, -1.0), -6.0, -1.0)
    a_log = jnp.clip(jax.random.uniform(key_of[5], (NS, WIDTH), jnp.float32, -1.0, 2.0), -1.0, 2.0)
    d_skip = jnp.clip(jax.random.uniform(key_of[6], (WIDTH,), jnp.float32, 0.5, 1.5), 0.5, 1.5)
    w_router = bell_draw(key_of[7], (EXPERTS, WIDTH), WIDTH ** -0.5, 0.09375)
    expert_ids_keys = jax.random.split(jax.random.fold_in(key_of[8], 1), RECORDS * LENGTH // TOK)
    expert_ids_turns = jax.random.permutation(jax.random.fold_in(key_of[8], 3), RECORDS * LENGTH // TOK)
    expert_ids = jax.vmap(lambda own, number: deal_out(jax.random.fold_in(key_of[8], 2), own, number, TOK, EXPERTS, 2, CAP, 2))(expert_ids_keys, expert_ids_turns).reshape((RECORDS, LENGTH, 2))
    w_up = bell_draw(key_of[9], (N_EXP, WIDTH, EH), WIDTH ** -0.5, 0.09375, ((0, 32), (1, 16)))
    w_down = bell_draw(key_of[10], (N_EXP, EH, WIDTH), (2 * EH) ** -0.5, 0.15625, ((0, 32), (2, 16)))
    return {"x_act": x_act, "dt_low": dt_low, "b_c": b_c, "w_dt": w_dt, "dt_bias": dt_bias, "a_log": a_log, "d_skip": d_skip, "w_router": w_router, "expert_ids": expert_ids, "w_up": w_up, "w_down": w_down}


def reference(x_act, dt_low, b_c, w_dt, dt_bias, a_log, d_skip, w_router, expert_ids, w_up, w_down):
    records, length, channels = x_act.shape
    low_rank = dt_low.shape[2]
    nstate = a_log.shape[0]
    pre = jnp.dot(dt_low.reshape(-1, low_rank), w_dt, preferred_element_type=jnp.float32)
    delta = jax.nn.softplus(pre.reshape(records, length, channels) + dt_bias)
    a_neg = -jnp.exp(a_log)
    xfloat = x_act.astype(jnp.float32)
    b_in = b_c[:, :, :nstate]
    c_out = b_c[:, :, nstate:]

    def advance(state, inputs):
        rate, driven, b_row, c_row = inputs
        state = jnp.exp(a_neg[None] * rate[:, None, :]) * state + driven[:, None, :] * b_row[:, :, None]
        return state, jnp.sum(c_row[:, :, None] * state, axis=1)

    start = jnp.zeros((records, nstate, channels), jnp.float32)
    _, outputs = lax.scan(advance, start, (jnp.swapaxes(delta, 0, 1), jnp.swapaxes(delta * xfloat, 0, 1), jnp.swapaxes(b_in, 0, 1), jnp.swapaxes(c_out, 0, 1)))
    scanned = jnp.swapaxes(outputs, 0, 1)
    mixer = (scanned + d_skip * xfloat).astype(jnp.bfloat16)

    rows_all = mixer.reshape(-1, channels)
    logits = jnp.dot(rows_all, w_router.T, preferred_element_type=jnp.float32)
    picks = expert_ids.reshape(-1, 2)
    chosen = jnp.take_along_axis(logits, picks, axis=1)
    first = jax.nn.sigmoid(chosen[:, 0] - chosen[:, 1])
    second = 1.0 - first
    blocks = rows_all.shape[0] // TOK
    pair_expert = picks.reshape(blocks, 2 * TOK)
    onehot = (pair_expert[:, :, None] == jnp.arange(EXPERTS, dtype=jnp.int32)[None, None, :]).astype(jnp.int32)
    position = jnp.sum(onehot * jnp.cumsum(onehot, axis=1), axis=2) - 1
    block_ids = jnp.broadcast_to(jnp.arange(blocks, dtype=jnp.int32)[:, None], (blocks, 2 * TOK))
    token_rows = block_ids * TOK + (jnp.arange(2 * TOK, dtype=jnp.int32) // 2)[None, :]
    table = jnp.zeros((blocks, EXPERTS, CAP), jnp.int32).at[block_ids, pair_expert, position].set(token_rows)

    def one_expert(index):
        rows = rows_all[table[:, index, :].reshape(-1)]
        total = jnp.zeros((rows.shape[0], channels), jnp.float32)
        for half in range(2):
            owner = 2 * index + half
            hidden = jax.nn.silu(jnp.dot(rows, w_up[owner], preferred_element_type=jnp.float32)).astype(jnp.bfloat16)
            partial_out = lax.optimization_barrier(jnp.dot(hidden, w_down[owner], preferred_element_type=jnp.float32).astype(jnp.bfloat16))
            total = total + partial_out.astype(jnp.float32)
        return total.astype(jnp.bfloat16)

    stacked = lax.map(one_expert, jnp.arange(EXPERTS, dtype=jnp.int32))
    flat_slot = block_ids * CAP + position
    picked = stacked[pair_expert.reshape(-1), flat_slot.reshape(-1)].reshape(-1, 2, channels).astype(jnp.float32)
    routed = first[:, None] * picked[:, 0] + second[:, None] * picked[:, 1]
    result = (rows_all.astype(jnp.float32) + routed).astype(jnp.bfloat16)
    return result.reshape(records, length, channels)
```

```python
import jax
import jax.numpy as jnp
from jax import lax
from jax.sharding import PartitionSpec as P


def from_behind(value, axis, by):
    count = lax.axis_size(axis)
    pairs = [(i, i + by) for i in range(count) if 0 <= i + by < count]
    return lax.ppermute(value, axis, pairs)


def carry_in(a_neg, total_delta, end_state):
    count = lax.axis_size("seq")
    packed = from_behind(jnp.concatenate([total_delta[None], end_state], axis=0), "seq", 1)
    covered = 1
    while covered < count - 1:
        older = from_behind(packed, "seq", covered)
        mine = packed[0]
        state = jnp.exp(a_neg * mine[None, :]) * older[1:] + packed[1:]
        packed = jnp.concatenate([(older[0] + mine)[None], state], axis=0)
        covered *= 2
    return packed[1:]


def sweep(start_state, a_neg, delta, driven, b_in, c_out):
    tokens_here, channels = delta.shape
    nstate = b_in.shape[1]
    group = 8
    turns = tokens_here // group

    def advance(state, inputs):
        rate, drive, b_rows, c_rows = inputs
        results = []
        for inner in range(group):
            state = (
                jnp.exp(a_neg * rate[inner][None, :]) * state
                + drive[inner][None, :] * b_rows[inner][:, None]
            )
            results.append(jnp.sum(c_rows[inner][:, None] * state, axis=0))
        return (state, jnp.stack(results))

    inputs = (
        delta.reshape(turns, group, channels),
        driven.reshape(turns, group, channels),
        b_in.reshape(turns, group, nstate),
        c_out.reshape(turns, group, nstate),
    )
    final, results = lax.scan(advance, start_state, inputs)
    return (final, results.reshape(tokens_here, channels))


def per_device(
    x_act, dt_low, b_c, w_dt, dt_bias, a_log, d_skip, w_router, expert_ids, w_up, w_down
):
    tokens_here = x_act.shape[1]
    channels = x_act.shape[2]
    nstate = a_log.shape[0]
    xfloat = x_act[0].astype(jnp.float32)
    pre = jnp.dot(dt_low[0], w_dt, preferred_element_type=jnp.float32)
    delta = jax.nn.softplus(pre + dt_bias)
    a_neg = -jnp.exp(a_log)
    driven = delta * xfloat
    b_in = b_c[0, :, :nstate]
    c_out = b_c[0, :, nstate:]
    cumulated = jnp.cumsum(delta, axis=0)
    pieces = max(1, channels // 512)
    span = channels // pieces
    ends = []
    for lower in range(0, channels, span):
        exponent = a_neg[None, :, lower : lower + span] * (
            cumulated[-1, lower : lower + span][None, None, :]
            - cumulated[:, None, lower : lower + span]
        )
        ends.append(
            jnp.sum(
                jnp.exp(exponent) * driven[:, None, lower : lower + span] * b_in[:, :, None], axis=0
            )
        )
    start = carry_in(a_neg, cumulated[-1], jnp.concatenate(ends, axis=1))
    _, scanned = sweep(start, a_neg, delta, driven, b_in, c_out)
    mixer = (scanned + d_skip * xfloat).astype(jnp.bfloat16)
    experts_count = w_router.shape[0]
    owners = lax.axis_size("exp")
    capacity = 5 * tokens_here // owners
    picks = expert_ids[0]
    logits = jnp.dot(mixer, w_router.T, preferred_element_type=jnp.float32)
    chosen = jnp.take_along_axis(logits, picks, axis=1)
    first = jax.nn.sigmoid(chosen[:, 0] - chosen[:, 1])
    second = 1.0 - first
    flat_ids = picks.reshape(-1)
    onehot = (flat_ids[:, None] == jnp.arange(experts_count, dtype=jnp.int32)[None, :]).astype(
        jnp.int32
    )
    position = (jnp.sum(onehot * jnp.cumsum(onehot, axis=0), axis=1) - 1).reshape(tokens_here, 2)
    halves = owners // experts_count
    dest = jnp.arange(owners, dtype=jnp.int32)[:, None, None] // halves
    slot = jnp.arange(capacity, dtype=jnp.int32)[None, :, None]
    hit = [
        (dest == picks[None, None, :, c]) & (slot == position[None, None, :, c]) for c in range(2)
    ]
    dispatch = (hit[0] | hit[1]).astype(jnp.bfloat16)
    outgoing = jnp.einsum(
        "jst,tc->jsc", dispatch, mixer, preferred_element_type=jnp.float32
    ).astype(jnp.bfloat16)
    incoming = lax.all_to_all(outgoing, "exp", split_axis=0, concat_axis=0, tiled=True)
    pre_hidden = jnp.einsum(
        "jsc,ch->jsh",
        incoming,
        lax.all_gather(w_up, "seq", axis=1, tiled=True)[0],
        preferred_element_type=jnp.float32,
    )
    hidden = jax.nn.silu(pre_hidden).astype(jnp.bfloat16)
    partial_out = lax.optimization_barrier(
        jnp.einsum(
            "jsh,hc->jsc",
            hidden,
            lax.all_gather(w_down, "seq", axis=2, tiled=True)[0],
            preferred_element_type=jnp.float32,
        ).astype(jnp.bfloat16)
    )
    returned = lax.all_to_all(partial_out, "exp", split_axis=0, concat_axis=0, tiled=True)
    gather = jnp.stack(hit).astype(jnp.bfloat16)
    picked = jnp.einsum(
        "kjst,jsc->ktc", gather, returned, preferred_element_type=jnp.float32
    ).astype(jnp.bfloat16).astype(jnp.float32)
    routed = first[:, None] * picked[0] + second[:, None] * picked[1]
    return (mixer.astype(jnp.float32) + routed).astype(jnp.bfloat16)[None]


def solution(mesh):
    in_specs = (
        P("exp", "seq", None),
        P("exp", "seq", None),
        P("exp", "seq", None),
        P(),
        P(),
        P(),
        P(),
        P(),
        P("exp", "seq", None),
        P("exp", "seq", None),
        P("exp", None, "seq"),
    )
    out_specs = P("exp", "seq", None)
    return jax.shard_map(
        per_device, mesh=mesh, in_specs=in_specs, out_specs=out_specs, check_vma=False
    )
```

```python
import jax
import jax.numpy as jnp
from jax import lax
from jax.sharding import PartitionSpec as P


def from_behind(value, axis, by):
    count = lax.axis_size(axis)
    pairs = [(i, i + by) for i in range(count) if 0 <= i + by < count]
    return lax.ppermute(value, axis, pairs)


def carry_in(a_neg, total_delta, end_state):
    count = lax.axis_size("seq")
    packed = from_behind(jnp.concatenate([total_delta[None], end_state], axis=0), "seq", 1)
    covered = 1
    while covered < count - 1:
        older = from_behind(packed, "seq", covered)
        mine = packed[0]
        state = jnp.exp(a_neg * mine[None, :]) * older[1:] + packed[1:]
        packed = jnp.concatenate([(older[0] + mine)[None], state], axis=0)
        covered *= 2
    return packed[1:]


def sweep(start_state, a_neg, delta, driven, b_in, c_out):
    tokens_here, channels = delta.shape
    nstate = b_in.shape[1]
    group = 32
    turns = tokens_here // group

    def advance(state, inputs):
        rate, drive, b_rows, c_rows = inputs
        results = []
        for inner in range(group):
            state = (
                jnp.exp(a_neg * rate[inner][None, :]) * state
                + drive[inner][None, :] * b_rows[inner][:, None]
            )
            results.append(jnp.sum(c_rows[inner][:, None] * state, axis=0))
        return (state, jnp.stack(results))

    inputs = (
        delta.reshape(turns, group, channels),
        driven.reshape(turns, group, channels),
        b_in.reshape(turns, group, nstate),
        c_out.reshape(turns, group, nstate),
    )
    final, results = lax.scan(advance, start_state, inputs)
    return (final, results.reshape(tokens_here, channels))


def per_device(
    x_act, dt_low, b_c, w_dt, dt_bias, a_log, d_skip, w_router, expert_ids, w_up, w_down
):
    tokens_here = x_act.shape[1]
    channels = x_act.shape[2]
    nstate = a_log.shape[0]
    xfloat = x_act[0].astype(jnp.float32)
    pre = jnp.dot(dt_low[0], w_dt, preferred_element_type=jnp.float32)
    delta = jax.nn.softplus(pre + dt_bias)
    a_neg = -jnp.exp(a_log)
    driven = delta * xfloat
    b_in = b_c[0, :, :nstate]
    c_out = b_c[0, :, nstate:]
    cumulated = jnp.cumsum(delta, axis=0)
    pieces = max(1, channels // 512)
    span = channels // pieces
    ends = []
    for lower in range(0, channels, span):
        exponent = a_neg[None, :, lower : lower + span] * (
            cumulated[-1, lower : lower + span][None, None, :]
            - cumulated[:, None, lower : lower + span]
        )
        ends.append(
            jnp.sum(
                jnp.exp(exponent) * driven[:, None, lower : lower + span] * b_in[:, :, None], axis=0
            )
        )
    start = carry_in(a_neg, cumulated[-1], jnp.concatenate(ends, axis=1))
    start, w_up, w_down = lax.optimization_barrier((start, w_up, w_down))
    _, scanned = sweep(start, a_neg, delta, driven, b_in, c_out)
    mixer = (scanned + d_skip * xfloat).astype(jnp.bfloat16)
    experts_count = w_router.shape[0]
    owners = lax.axis_size("exp")
    capacity = 5 * tokens_here // owners
    picks = expert_ids[0]
    logits = jnp.dot(mixer, w_router.T, preferred_element_type=jnp.float32)
    chosen = jnp.take_along_axis(logits, picks, axis=1)
    first = jax.nn.sigmoid(chosen[:, 0] - chosen[:, 1])
    second = 1.0 - first
    flat_ids = picks.reshape(-1)
    onehot = (flat_ids[:, None] == jnp.arange(experts_count, dtype=jnp.int32)[None, :]).astype(
        jnp.int32
    )
    position = (jnp.sum(onehot * jnp.cumsum(onehot, axis=0), axis=1) - 1).reshape(tokens_here, 2)
    halves = owners // experts_count
    dest = jnp.arange(owners, dtype=jnp.int32)[:, None, None] // halves
    slot = jnp.arange(capacity, dtype=jnp.int32)[None, :, None]
    hit = [
        (dest == picks[None, None, :, c]) & (slot == position[None, None, :, c]) for c in range(2)
    ]
    dispatch = (hit[0] | hit[1]).astype(jnp.bfloat16)
    outgoing = jnp.einsum(
        "jst,tc->jsc", dispatch, mixer, preferred_element_type=jnp.float32
    ).astype(jnp.bfloat16)
    incoming = lax.all_to_all(outgoing, "exp", split_axis=0, concat_axis=0, tiled=True)
    pre_hidden = jnp.einsum(
        "jsc,ch->jsh",
        incoming,
        lax.all_gather(w_up, "seq", axis=1, tiled=True)[0],
        preferred_element_type=jnp.float32,
    )
    hidden = jax.nn.silu(pre_hidden).astype(jnp.bfloat16)
    partial_out = lax.optimization_barrier(
        jnp.einsum(
            "jsh,hc->jsc",
            hidden,
            lax.all_gather(w_down, "seq", axis=2, tiled=True)[0],
            preferred_element_type=jnp.float32,
        ).astype(jnp.bfloat16)
    )
    returned = lax.all_to_all(partial_out, "exp", split_axis=0, concat_axis=0, tiled=True)
    gather = jnp.stack(hit).astype(jnp.bfloat16)
    picked = jnp.einsum(
        "kjst,jsc->ktc", gather, returned, preferred_element_type=jnp.float32
    ).astype(jnp.bfloat16).astype(jnp.float32)
    routed = first[:, None] * picked[0] + second[:, None] * picked[1]
    return (mixer.astype(jnp.float32) + routed).astype(jnp.bfloat16)[None]


def solution(mesh):
    in_specs = (
        P("exp", "seq", None),
        P("exp", "seq", None),
        P("exp", "seq", None),
        P(),
        P(),
        P(),
        P(),
        P(),
        P("exp", "seq", None),
        P("exp", "seq", None),
        P("exp", None, "seq"),
    )
    out_specs = P("exp", "seq", None)
    return jax.shard_map(
        per_device, mesh=mesh, in_specs=in_specs, out_specs=out_specs, check_vma=False
    )
```

```python
import jax
import jax.numpy as jnp
from jax import lax
from jax.experimental import pallas as pl
from jax.sharding import PartitionSpec as P


def from_behind(value, axis, by):
    count = lax.axis_size(axis)
    pairs = [(i, i + by) for i in range(count) if 0 <= i + by < count]
    return lax.ppermute(value, axis, pairs)


def carry_in(a_neg, total_delta, end_state):
    count = lax.axis_size("seq")
    packed = from_behind(jnp.concatenate([total_delta[None], end_state], axis=0), "seq", 1)
    covered = 1
    while covered < count - 1:
        older = from_behind(packed, "seq", covered)
        mine = packed[0]
        state = jnp.exp(a_neg * mine[None, :]) * older[1:] + packed[1:]
        packed = jnp.concatenate([(older[0] + mine)[None], state], axis=0)
        covered *= 2
    return packed[1:]


def sweep_kernel(delta_ref, driven_ref, a_ref, start_ref, b_ref, c_ref, y_ref):
    tokens_here = delta_ref.shape[0]
    lanes = b_ref.shape[2]
    subs = delta_ref.shape[1] // lanes
    rates = [a_ref[:, i * lanes : (i + 1) * lanes] for i in range(subs)]

    def step(t, states):
        b_rows = b_ref[t]
        c_rows = c_ref[t]
        d_row = delta_ref[pl.ds(t, 1), :]
        u_row = driven_ref[pl.ds(t, 1), :]
        new_states = []
        outs = []
        for i in range(subs):
            d = d_row[:, i * lanes : (i + 1) * lanes]
            u = u_row[:, i * lanes : (i + 1) * lanes]
            state = jnp.exp(rates[i] * d) * states[i] + u * b_rows
            new_states.append(state)
            outs.append(jnp.sum(c_rows * state, axis=0, keepdims=True))
        y_ref[pl.ds(t, 1), :] = jnp.concatenate(outs, axis=1)
        return tuple(new_states)

    first = tuple(start_ref[:, i * lanes : (i + 1) * lanes] for i in range(subs))
    lax.fori_loop(0, tokens_here, step, first, unroll=8)


def sweep(start_state, a_neg, delta, driven, b_in, c_out):
    tokens_here, channels = delta.shape
    nstate = b_in.shape[1]
    lanes = 128
    block = 512
    b_wide = jnp.broadcast_to(b_in[:, :, None], (tokens_here, nstate, lanes))
    c_wide = jnp.broadcast_to(c_out[:, :, None], (tokens_here, nstate, lanes))
    row_spec = pl.BlockSpec((tokens_here, block), lambda k: (0, k))
    state_spec = pl.BlockSpec((nstate, block), lambda k: (0, k))
    wide_spec = pl.BlockSpec((tokens_here, nstate, lanes), lambda k: (0, 0, 0))
    return pl.pallas_call(
        sweep_kernel,
        out_shape=jax.ShapeDtypeStruct((tokens_here, channels), jnp.float32),
        grid=(channels // block,),
        in_specs=[row_spec, row_spec, state_spec, state_spec, wide_spec, wide_spec],
        out_specs=row_spec,
        cost_estimate=pl.CostEstimate(
            flops=8 * tokens_here * nstate * channels,
            transcendentals=tokens_here * nstate * channels,
            bytes_accessed=4 * (3 * tokens_here * channels + 2 * nstate * channels),
        ),
    )(delta, driven, a_neg, start_state, b_wide, c_wide)


def per_device(
    x_act, dt_low, b_c, w_dt, dt_bias, a_log, d_skip, w_router, expert_ids, w_up, w_down
):
    tokens_here = x_act.shape[1]
    channels = x_act.shape[2]
    nstate = a_log.shape[0]
    xfloat = x_act[0].astype(jnp.float32)
    pre = jnp.dot(dt_low[0], w_dt, preferred_element_type=jnp.float32)
    delta = jax.nn.softplus(pre + dt_bias)
    a_neg = -jnp.exp(a_log)
    driven = delta * xfloat
    b_in = b_c[0, :, :nstate]
    c_out = b_c[0, :, nstate:]
    cumulated = jnp.cumsum(delta, axis=0)
    pieces = max(1, channels // 512)
    span = channels // pieces
    ends = []
    for lower in range(0, channels, span):
        exponent = a_neg[None, :, lower : lower + span] * (
            cumulated[-1, lower : lower + span][None, None, :]
            - cumulated[:, None, lower : lower + span]
        )
        ends.append(
            jnp.sum(
                jnp.exp(exponent) * driven[:, None, lower : lower + span] * b_in[:, :, None], axis=0
            )
        )
    start = carry_in(a_neg, cumulated[-1], jnp.concatenate(ends, axis=1))
    start, w_up, w_down = lax.optimization_barrier((start, w_up, w_down))
    scanned = sweep(start, a_neg, delta, driven, b_in, c_out)
    mixer = (scanned + d_skip * xfloat).astype(jnp.bfloat16)
    experts_count = w_router.shape[0]
    owners = lax.axis_size("exp")
    capacity = 5 * tokens_here // owners
    picks = expert_ids[0]
    logits = jnp.dot(mixer, w_router.T, preferred_element_type=jnp.float32)
    chosen = jnp.take_along_axis(logits, picks, axis=1)
    first = jax.nn.sigmoid(chosen[:, 0] - chosen[:, 1])
    second = 1.0 - first
    flat_ids = picks.reshape(-1)
    onehot = (flat_ids[:, None] == jnp.arange(experts_count, dtype=jnp.int32)[None, :]).astype(
        jnp.int32
    )
    position = (jnp.sum(onehot * jnp.cumsum(onehot, axis=0), axis=1) - 1).reshape(tokens_here, 2)
    halves = owners // experts_count
    dest = jnp.arange(owners, dtype=jnp.int32)[:, None, None] // halves
    slot = jnp.arange(capacity, dtype=jnp.int32)[None, :, None]
    hit = [
        (dest == picks[None, None, :, c]) & (slot == position[None, None, :, c]) for c in range(2)
    ]
    dispatch = (hit[0] | hit[1]).astype(jnp.bfloat16)
    outgoing = jnp.einsum(
        "jst,tc->jsc", dispatch, mixer, preferred_element_type=jnp.float32
    ).astype(jnp.bfloat16)
    incoming = lax.all_to_all(outgoing, "exp", split_axis=0, concat_axis=0, tiled=True)
    pre_hidden = jnp.einsum(
        "jsc,ch->jsh",
        incoming,
        lax.all_gather(w_up, "seq", axis=1, tiled=True)[0],
        preferred_element_type=jnp.float32,
    )
    hidden = jax.nn.silu(pre_hidden).astype(jnp.bfloat16)
    partial_out = lax.optimization_barrier(
        jnp.einsum(
            "jsh,hc->jsc",
            hidden,
            lax.all_gather(w_down, "seq", axis=2, tiled=True)[0],
            preferred_element_type=jnp.float32,
        ).astype(jnp.bfloat16)
    )
    returned = lax.all_to_all(partial_out, "exp", split_axis=0, concat_axis=0, tiled=True)
    gather = jnp.stack(hit).astype(jnp.bfloat16)
    picked = jnp.einsum(
        "kjst,jsc->ktc", gather, returned, preferred_element_type=jnp.float32
    ).astype(jnp.bfloat16).astype(jnp.float32)
    routed = first[:, None] * picked[0] + second[:, None] * picked[1]
    return (mixer.astype(jnp.float32) + routed).astype(jnp.bfloat16)[None]


def solution(mesh):
    in_specs = (
        P("exp", "seq", None),
        P("exp", "seq", None),
        P("exp", "seq", None),
        P(),
        P(),
        P(),
        P(),
        P(),
        P("exp", "seq", None),
        P("exp", "seq", None),
        P("exp", None, "seq"),
    )
    out_specs = P("exp", "seq", None)
    return jax.shard_map(
        per_device, mesh=mesh, in_specs=in_specs, out_specs=out_specs, check_vma=False
    )
```

```python
import jax
import jax.numpy as jnp
from jax import lax
from jax.experimental import pallas as pl
from jax.sharding import PartitionSpec as P


def from_behind(value, axis, by):
    count = lax.axis_size(axis)
    pairs = [(i, i + by) for i in range(count) if 0 <= i + by < count]
    return lax.ppermute(value, axis, pairs)


def carry_in(a_neg, total_delta, end_state):
    count = lax.axis_size("seq")
    packed = from_behind(jnp.concatenate([total_delta[None], end_state], axis=0), "seq", 1)
    covered = 1
    while covered < count - 1:
        older = from_behind(packed, "seq", covered)
        mine = packed[0]
        state = jnp.exp(a_neg * mine[None, :]) * older[1:] + packed[1:]
        packed = jnp.concatenate([(older[0] + mine)[None], state], axis=0)
        covered *= 2
    return packed[1:]


def sweep_kernel(delta_ref, driven_ref, a_ref, start_ref, b_ref, c_ref, y_ref):
    tokens_here = delta_ref.shape[0]
    lanes = b_ref.shape[2]
    subs = delta_ref.shape[1] // lanes
    rates = [a_ref[:, i * lanes : (i + 1) * lanes] for i in range(subs)]

    def step(t, states):
        b_rows = b_ref[t]
        c_rows = c_ref[t]
        d_row = delta_ref[pl.ds(t, 1), :]
        u_row = driven_ref[pl.ds(t, 1), :]
        new_states = []
        outs = []
        for i in range(subs):
            d = d_row[:, i * lanes : (i + 1) * lanes]
            u = u_row[:, i * lanes : (i + 1) * lanes]
            state = jnp.exp(rates[i] * d) * states[i] + u * b_rows
            new_states.append(state)
            outs.append(jnp.sum(c_rows * state, axis=0, keepdims=True))
        y_ref[pl.ds(t, 1), :] = jnp.concatenate(outs, axis=1)
        return tuple(new_states)

    first = tuple(start_ref[:, i * lanes : (i + 1) * lanes] for i in range(subs))
    lax.fori_loop(0, tokens_here, step, first, unroll=8)


def sweep(start_state, a_neg, delta, driven, b_in, c_out):
    tokens_here, channels = delta.shape
    nstate = b_in.shape[1]
    lanes = 128
    block = 512
    b_wide = jnp.broadcast_to(b_in[:, :, None], (tokens_here, nstate, lanes))
    c_wide = jnp.broadcast_to(c_out[:, :, None], (tokens_here, nstate, lanes))
    row_spec = pl.BlockSpec((tokens_here, block), lambda k: (0, k))
    state_spec = pl.BlockSpec((nstate, block), lambda k: (0, k))
    wide_spec = pl.BlockSpec((tokens_here, nstate, lanes), lambda k: (0, 0, 0))
    return pl.pallas_call(
        sweep_kernel,
        out_shape=jax.ShapeDtypeStruct((tokens_here, channels), jnp.float32),
        grid=(channels // block,),
        in_specs=[row_spec, row_spec, state_spec, state_spec, wide_spec, wide_spec],
        out_specs=row_spec,
        cost_estimate=pl.CostEstimate(
            flops=8 * tokens_here * nstate * channels,
            transcendentals=tokens_here * nstate * channels,
            bytes_accessed=4 * (3 * tokens_here * channels + 2 * nstate * channels),
        ),
    )(delta, driven, a_neg, start_state, b_wide, c_wide)


def per_device(
    x_act, dt_low, b_c, w_dt, dt_bias, a_log, d_skip, w_router, expert_ids, w_up, w_down
):
    tokens_here = x_act.shape[1]
    channels = x_act.shape[2]
    nstate = a_log.shape[0]
    xfloat = x_act[0].astype(jnp.float32)
    pre = jnp.dot(dt_low[0], w_dt, preferred_element_type=jnp.float32)
    delta = jax.nn.softplus(pre + dt_bias)
    a_neg = -jnp.exp(a_log)
    driven = delta * xfloat
    b_in = b_c[0, :, :nstate]
    c_out = b_c[0, :, nstate:]
    cumulated = jnp.cumsum(delta, axis=0)
    pieces = max(1, channels // 512)
    span = channels // pieces
    ends = []
    for lower in range(0, channels, span):
        exponent = a_neg[None, :, lower : lower + span] * (
            cumulated[-1, lower : lower + span][None, None, :]
            - cumulated[:, None, lower : lower + span]
        )
        ends.append(
            jnp.sum(
                jnp.exp(exponent) * driven[:, None, lower : lower + span] * b_in[:, :, None], axis=0
            )
        )
    start = carry_in(a_neg, cumulated[-1], jnp.concatenate(ends, axis=1))
    start, w_up, w_down = lax.optimization_barrier((start, w_up, w_down))
    scanned = sweep(start, a_neg, delta, driven, b_in, c_out)
    mixer = (scanned + d_skip * xfloat).astype(jnp.bfloat16)
    experts_count = w_router.shape[0]
    owners = lax.axis_size("exp")
    capacity = 5 * tokens_here // owners
    picks = expert_ids[0]
    logits = jnp.dot(mixer, w_router.T, preferred_element_type=jnp.float32)
    chosen = jnp.take_along_axis(logits, picks, axis=1)
    first = jax.nn.sigmoid(chosen[:, 0] - chosen[:, 1])
    second = 1.0 - first
    flat_ids = picks.reshape(-1)
    onehot = (flat_ids[:, None] == jnp.arange(experts_count, dtype=jnp.int32)[None, :]).astype(
        jnp.int32
    )
    position = (jnp.sum(onehot * jnp.cumsum(onehot, axis=0), axis=1) - 1).reshape(tokens_here, 2)
    halves = owners // experts_count
    dest = jnp.arange(owners, dtype=jnp.int32)[:, None, None] // halves
    slot = jnp.arange(capacity, dtype=jnp.int32)[None, :, None]
    hit = [
        (dest == picks[None, None, :, c]) & (slot == position[None, None, :, c]) for c in range(2)
    ]
    dispatch = (hit[0] | hit[1]).astype(jnp.bfloat16)
    gather = jnp.stack(hit).astype(jnp.bfloat16)
    w_up_full = lax.all_gather(w_up, "seq", axis=1, tiled=True)[0]
    w_down_full = lax.all_gather(w_down, "seq", axis=2, tiled=True)[0]
    chunks = 2
    step = capacity // chunks
    picked = None
    for lower in range(0, capacity, step):
        outgoing = jnp.einsum(
            "jst,tc->jsc", dispatch[:, lower : lower + step], mixer, preferred_element_type=jnp.float32
        ).astype(jnp.bfloat16)
        incoming = lax.all_to_all(outgoing, "exp", split_axis=0, concat_axis=0, tiled=True)
        pre_hidden = jnp.einsum(
            "jsc,ch->jsh", incoming, w_up_full, preferred_element_type=jnp.float32
        )
        hidden = jax.nn.silu(pre_hidden).astype(jnp.bfloat16)
        partial_out = lax.optimization_barrier(
            jnp.einsum(
                "jsh,hc->jsc", hidden, w_down_full, preferred_element_type=jnp.float32
            ).astype(jnp.bfloat16)
        )
        returned = lax.all_to_all(partial_out, "exp", split_axis=0, concat_axis=0, tiled=True)
        part = jnp.einsum(
            "kjst,jsc->ktc",
            gather[:, :, lower : lower + step],
            returned,
            preferred_element_type=jnp.float32,
        )
        picked = part if picked is None else picked + part
    picked = picked.astype(jnp.bfloat16).astype(jnp.float32)
    routed = first[:, None] * picked[0] + second[:, None] * picked[1]
    return (mixer.astype(jnp.float32) + routed).astype(jnp.bfloat16)[None]


def solution(mesh):
    in_specs = (
        P("exp", "seq", None),
        P("exp", "seq", None),
        P("exp", "seq", None),
        P(),
        P(),
        P(),
        P(),
        P(),
        P("exp", "seq", None),
        P("exp", "seq", None),
        P("exp", None, "seq"),
    )
    out_specs = P("exp", "seq", None)
    return jax.shard_map(
        per_device, mesh=mesh, in_specs=in_specs, out_specs=out_specs, check_vma=False
    )
```

```python
import jax
import jax.numpy as jnp
from jax import lax
from jax.experimental import pallas as pl
from jax.sharding import PartitionSpec as P


def from_behind(value, axis, by):
    count = lax.axis_size(axis)
    pairs = [(i, i + by) for i in range(count) if 0 <= i + by < count]
    return lax.ppermute(value, axis, pairs)


def compose(a_neg, older, newer):
    total = older[0] + newer[0]
    state = jnp.exp(a_neg * newer[0][None, :]) * older[1:] + newer[1:]
    return jnp.concatenate([total[None], state], axis=0)


def carry_in(a_neg, total_delta, end_state):
    count = lax.axis_size("seq")
    radix = 4
    packed = jnp.concatenate([total_delta[None], end_state], axis=0)
    pieces = [from_behind(packed, "seq", k) for k in range(radix, 0, -1)]
    covered = radix
    while True:
        merged = pieces[0]
        for piece in pieces[1:]:
            merged = compose(a_neg, merged, piece)
        if covered >= count - 1:
            return merged[1:]
        pieces = [from_behind(merged, "seq", k * covered) for k in range(radix - 1, 0, -1)]
        pieces.append(merged)
        covered *= radix


def sweep_kernel(delta_ref, driven_ref, a_ref, start_ref, b_ref, c_ref, y_ref):
    tokens_here = delta_ref.shape[0]
    lanes = b_ref.shape[2]
    subs = delta_ref.shape[1] // lanes
    rates = [a_ref[:, i * lanes : (i + 1) * lanes] for i in range(subs)]

    def step(t, states):
        b_rows = b_ref[t]
        c_rows = c_ref[t]
        d_row = delta_ref[pl.ds(t, 1), :]
        u_row = driven_ref[pl.ds(t, 1), :]
        new_states = []
        outs = []
        for i in range(subs):
            d = d_row[:, i * lanes : (i + 1) * lanes]
            u = u_row[:, i * lanes : (i + 1) * lanes]
            state = jnp.exp(rates[i] * d) * states[i] + u * b_rows
            new_states.append(state)
            outs.append(jnp.sum(c_rows * state, axis=0, keepdims=True))
        y_ref[pl.ds(t, 1), :] = jnp.concatenate(outs, axis=1)
        return tuple(new_states)

    first = tuple(start_ref[:, i * lanes : (i + 1) * lanes] for i in range(subs))
    lax.fori_loop(0, tokens_here, step, first, unroll=8)


def sweep(start_state, a_neg, delta, driven, b_in, c_out):
    tokens_here, channels = delta.shape
    nstate = b_in.shape[1]
    lanes = 128
    block = 512
    b_wide = jnp.broadcast_to(b_in[:, :, None], (tokens_here, nstate, lanes))
    c_wide = jnp.broadcast_to(c_out[:, :, None], (tokens_here, nstate, lanes))
    row_spec = pl.BlockSpec((tokens_here, block), lambda k: (0, k))
    state_spec = pl.BlockSpec((nstate, block), lambda k: (0, k))
    wide_spec = pl.BlockSpec((tokens_here, nstate, lanes), lambda k: (0, 0, 0))
    return pl.pallas_call(
        sweep_kernel,
        out_shape=jax.ShapeDtypeStruct((tokens_here, channels), jnp.float32),
        grid=(channels // block,),
        in_specs=[row_spec, row_spec, state_spec, state_spec, wide_spec, wide_spec],
        out_specs=row_spec,
        cost_estimate=pl.CostEstimate(
            flops=8 * tokens_here * nstate * channels,
            transcendentals=tokens_here * nstate * channels,
            bytes_accessed=4 * (3 * tokens_here * channels + 2 * nstate * channels),
        ),
    )(delta, driven, a_neg, start_state, b_wide, c_wide)


def per_device(
    x_act, dt_low, b_c, w_dt, dt_bias, a_log, d_skip, w_router, expert_ids, w_up, w_down
):
    tokens_here = x_act.shape[1]
    channels = x_act.shape[2]
    nstate = a_log.shape[0]
    xfloat = x_act[0].astype(jnp.float32)
    pre = jnp.dot(dt_low[0], w_dt, preferred_element_type=jnp.float32)
    delta = jax.nn.softplus(pre + dt_bias)
    a_neg = -jnp.exp(a_log)
    driven = delta * xfloat
    b_in = b_c[0, :, :nstate]
    c_out = b_c[0, :, nstate:]
    cumulated = jnp.cumsum(delta, axis=0)
    pieces = max(1, channels // 512)
    span = channels // pieces
    ends = []
    for lower in range(0, channels, span):
        exponent = a_neg[None, :, lower : lower + span] * (
            cumulated[-1, lower : lower + span][None, None, :]
            - cumulated[:, None, lower : lower + span]
        )
        ends.append(
            jnp.sum(
                jnp.exp(exponent) * driven[:, None, lower : lower + span] * b_in[:, :, None], axis=0
            )
        )
    start = carry_in(a_neg, cumulated[-1], jnp.concatenate(ends, axis=1))
    start, w_up, w_down = lax.optimization_barrier((start, w_up, w_down))
    scanned = sweep(start, a_neg, delta, driven, b_in, c_out)
    mixer = (scanned + d_skip * xfloat).astype(jnp.bfloat16)
    experts_count = w_router.shape[0]
    owners = lax.axis_size("exp")
    capacity = 5 * tokens_here // owners
    picks = expert_ids[0]
    logits = jnp.dot(mixer, w_router.T, preferred_element_type=jnp.float32)
    chosen = jnp.take_along_axis(logits, picks, axis=1)
    first = jax.nn.sigmoid(chosen[:, 0] - chosen[:, 1])
    second = 1.0 - first
    flat_ids = picks.reshape(-1)
    onehot = (flat_ids[:, None] == jnp.arange(experts_count, dtype=jnp.int32)[None, :]).astype(
        jnp.int32
    )
    position = (jnp.sum(onehot * jnp.cumsum(onehot, axis=0), axis=1) - 1).reshape(tokens_here, 2)
    halves = owners // experts_count
    dest = jnp.arange(owners, dtype=jnp.int32)[:, None, None] // halves
    slot = jnp.arange(capacity, dtype=jnp.int32)[None, :, None]
    hit = [
        (dest == picks[None, None, :, c]) & (slot == position[None, None, :, c]) for c in range(2)
    ]
    rows_out = owners * capacity
    dispatch = (hit[0] | hit[1]).astype(jnp.bfloat16).reshape(rows_out, tokens_here)
    outgoing = jnp.dot(dispatch, mixer, preferred_element_type=jnp.float32).astype(jnp.bfloat16)
    incoming = lax.all_to_all(outgoing, "exp", split_axis=0, concat_axis=0, tiled=True)
    pre_hidden = jnp.dot(
        incoming,
        lax.all_gather(w_up, "seq", axis=1, tiled=True)[0],
        preferred_element_type=jnp.float32,
    )
    hidden = jax.nn.silu(pre_hidden).astype(jnp.bfloat16)
    partial_out = lax.optimization_barrier(
        jnp.dot(
            hidden,
            lax.all_gather(w_down, "seq", axis=2, tiled=True)[0],
            preferred_element_type=jnp.float32,
        ).astype(jnp.bfloat16)
    )
    returned = lax.all_to_all(partial_out, "exp", split_axis=0, concat_axis=0, tiled=True)
    gather = jnp.stack(hit).astype(jnp.bfloat16).reshape(2, rows_out, tokens_here)
    picked = jnp.einsum(
        "kqt,qc->ktc", gather, returned, preferred_element_type=jnp.float32
    ).astype(jnp.bfloat16).astype(jnp.float32)
    routed = first[:, None] * picked[0] + second[:, None] * picked[1]
    return (mixer.astype(jnp.float32) + routed).astype(jnp.bfloat16)[None]


def solution(mesh):
    in_specs = (
        P("exp", "seq", None),
        P("exp", "seq", None),
        P("exp", "seq", None),
        P(),
        P(),
        P(),
        P(),
        P(),
        P("exp", "seq", None),
        P("exp", "seq", None),
        P("exp", None, "seq"),
    )
    out_specs = P("exp", "seq", None)
    return jax.shard_map(
        per_device, mesh=mesh, in_specs=in_specs, out_specs=out_specs, check_vma=False
    )
```

```python
import jax
import jax.numpy as jnp
from jax import lax
from jax.experimental import pallas as pl
from jax.sharding import PartitionSpec as P


def from_behind(value, axis, by):
    count = lax.axis_size(axis)
    pairs = [(i, i + by) for i in range(count) if 0 <= i + by < count]
    return lax.ppermute(value, axis, pairs)


def carry_in(a_neg, total_delta, end_state):
    count = lax.axis_size("seq")
    me = lax.axis_index("seq")
    packed = jnp.concatenate([total_delta[None], end_state], axis=0)
    every = lax.all_gather(packed, "seq")
    state = jnp.zeros_like(end_state)
    for k in range(count - 1):
        folded = jnp.exp(a_neg * every[k, 0][None, :]) * state + every[k, 1:]
        state = jnp.where(k < me, folded, state)
    return state


def sweep_kernel(delta_ref, driven_ref, a_ref, start_ref, b_ref, c_ref, y_ref):
    tokens_here = delta_ref.shape[0]
    lanes = b_ref.shape[2]
    subs = delta_ref.shape[1] // lanes
    rates = [a_ref[:, i * lanes : (i + 1) * lanes] for i in range(subs)]

    def step(t, states):
        b_rows = b_ref[t]
        c_rows = c_ref[t]
        d_row = delta_ref[pl.ds(t, 1), :]
        u_row = driven_ref[pl.ds(t, 1), :]
        new_states = []
        outs = []
        for i in range(subs):
            d = d_row[:, i * lanes : (i + 1) * lanes]
            u = u_row[:, i * lanes : (i + 1) * lanes]
            state = jnp.exp(rates[i] * d) * states[i] + u * b_rows
            new_states.append(state)
            outs.append(jnp.sum(c_rows * state, axis=0, keepdims=True))
        y_ref[pl.ds(t, 1), :] = jnp.concatenate(outs, axis=1)
        return tuple(new_states)

    first = tuple(start_ref[:, i * lanes : (i + 1) * lanes] for i in range(subs))
    lax.fori_loop(0, tokens_here, step, first, unroll=8)


def sweep(start_state, a_neg, delta, driven, b_in, c_out):
    tokens_here, channels = delta.shape
    nstate = b_in.shape[1]
    lanes = 128
    block = 512
    b_wide = jnp.broadcast_to(b_in[:, :, None], (tokens_here, nstate, lanes))
    c_wide = jnp.broadcast_to(c_out[:, :, None], (tokens_here, nstate, lanes))
    row_spec = pl.BlockSpec((tokens_here, block), lambda k: (0, k))
    state_spec = pl.BlockSpec((nstate, block), lambda k: (0, k))
    wide_spec = pl.BlockSpec((tokens_here, nstate, lanes), lambda k: (0, 0, 0))
    return pl.pallas_call(
        sweep_kernel,
        out_shape=jax.ShapeDtypeStruct((tokens_here, channels), jnp.float32),
        grid=(channels // block,),
        in_specs=[row_spec, row_spec, state_spec, state_spec, wide_spec, wide_spec],
        out_specs=row_spec,
        cost_estimate=pl.CostEstimate(
            flops=8 * tokens_here * nstate * channels,
            transcendentals=tokens_here * nstate * channels,
            bytes_accessed=4 * (3 * tokens_here * channels + 2 * nstate * channels),
        ),
    )(delta, driven, a_neg, start_state, b_wide, c_wide)


def per_device(
    x_act, dt_low, b_c, w_dt, dt_bias, a_log, d_skip, w_router, expert_ids, w_up, w_down
):
    tokens_here = x_act.shape[1]
    channels = x_act.shape[2]
    nstate = a_log.shape[0]
    xfloat = x_act[0].astype(jnp.float32)
    pre = jnp.dot(dt_low[0], w_dt, preferred_element_type=jnp.float32)
    delta = jax.nn.softplus(pre + dt_bias)
    a_neg = -jnp.exp(a_log)
    driven = delta * xfloat
    b_in = b_c[0, :, :nstate]
    c_out = b_c[0, :, nstate:]
    cumulated = jnp.cumsum(delta, axis=0)
    pieces = max(1, channels // 512)
    span = channels // pieces
    ends = []
    for lower in range(0, channels, span):
        exponent = a_neg[None, :, lower : lower + span] * (
            cumulated[-1, lower : lower + span][None, None, :]
            - cumulated[:, None, lower : lower + span]
        )
        ends.append(
            jnp.sum(
                jnp.exp(exponent) * driven[:, None, lower : lower + span] * b_in[:, :, None], axis=0
            )
        )
    start = carry_in(a_neg, cumulated[-1], jnp.concatenate(ends, axis=1))
    start, w_up, w_down = lax.optimization_barrier((start, w_up, w_down))
    scanned = sweep(start, a_neg, delta, driven, b_in, c_out)
    mixer = (scanned + d_skip * xfloat).astype(jnp.bfloat16)
    experts_count = w_router.shape[0]
    owners = lax.axis_size("exp")
    capacity = 5 * tokens_here // owners
    picks = expert_ids[0]
    logits = jnp.dot(mixer, w_router.T, preferred_element_type=jnp.float32)
    chosen = jnp.take_along_axis(logits, picks, axis=1)
    first = jax.nn.sigmoid(chosen[:, 0] - chosen[:, 1])
    second = 1.0 - first
    flat_ids = picks.reshape(-1)
    onehot = (flat_ids[:, None] == jnp.arange(experts_count, dtype=jnp.int32)[None, :]).astype(
        jnp.int32
    )
    position = (jnp.sum(onehot * jnp.cumsum(onehot, axis=0), axis=1) - 1).reshape(tokens_here, 2)
    halves = owners // experts_count
    dest = jnp.arange(owners, dtype=jnp.int32)[:, None, None] // halves
    slot = jnp.arange(capacity, dtype=jnp.int32)[None, :, None]
    hit = [
        (dest == picks[None, None, :, c]) & (slot == position[None, None, :, c]) for c in range(2)
    ]
    dispatch = (hit[0] | hit[1]).astype(jnp.bfloat16)
    outgoing = jnp.einsum(
        "jst,tc->jsc", dispatch, mixer, preferred_element_type=jnp.float32
    ).astype(jnp.bfloat16)
    incoming = lax.all_to_all(outgoing, "exp", split_axis=0, concat_axis=0, tiled=True)
    pre_hidden = jnp.einsum(
        "jsc,ch->jsh",
        incoming,
        lax.all_gather(w_up, "seq", axis=1, tiled=True)[0],
        preferred_element_type=jnp.float32,
    )
    hidden = jax.nn.silu(pre_hidden).astype(jnp.bfloat16)
    partial_out = lax.optimization_barrier(
        jnp.einsum(
            "jsh,hc->jsc",
            hidden,
            lax.all_gather(w_down, "seq", axis=2, tiled=True)[0],
            preferred_element_type=jnp.float32,
        ).astype(jnp.bfloat16)
    )
    returned = lax.all_to_all(partial_out, "exp", split_axis=0, concat_axis=0, tiled=True)
    gather = jnp.stack(hit).astype(jnp.bfloat16)
    picked = jnp.einsum(
        "kjst,jsc->ktc", gather, returned, preferred_element_type=jnp.float32
    ).astype(jnp.bfloat16).astype(jnp.float32)
    routed = first[:, None] * picked[0] + second[:, None] * picked[1]
    return (mixer.astype(jnp.float32) + routed).astype(jnp.bfloat16)[None]


def solution(mesh):
    in_specs = (
        P("exp", "seq", None),
        P("exp", "seq", None),
        P("exp", "seq", None),
        P(),
        P(),
        P(),
        P(),
        P(),
        P("exp", "seq", None),
        P("exp", "seq", None),
        P("exp", None, "seq"),
    )
    out_specs = P("exp", "seq", None)
    return jax.shard_map(
        per_device, mesh=mesh, in_specs=in_specs, out_specs=out_specs, check_vma=False
    )
```

```python
import jax
import jax.numpy as jnp
from jax import lax
from jax.experimental import pallas as pl
from jax.sharding import PartitionSpec as P


def from_behind(value, axis, by):
    count = lax.axis_size(axis)
    pairs = [(i, i + by) for i in range(count) if 0 <= i + by < count]
    return lax.ppermute(value, axis, pairs)


def carry_in(a_neg, total_delta, end_state):
    count = lax.axis_size("seq")
    me = lax.axis_index("seq")
    packed = jnp.concatenate([total_delta[None], end_state], axis=0)
    every = lax.all_gather(packed, "seq")
    state = jnp.zeros_like(end_state)
    for k in range(count - 1):
        folded = jnp.exp(a_neg * every[k, 0][None, :]) * state + every[k, 1:]
        state = jnp.where(k < me, folded, state)
    return state


def sweep_kernel(delta_ref, driven_ref, a_ref, start_ref, b_ref, c_ref, y_ref):
    tokens_here = delta_ref.shape[0]
    lanes = b_ref.shape[2]
    subs = delta_ref.shape[1] // lanes
    rates = [a_ref[:, i * lanes : (i + 1) * lanes] for i in range(subs)]

    def step(t, states):
        b_rows = b_ref[t]
        c_rows = c_ref[t]
        d_row = delta_ref[pl.ds(t, 1), :]
        u_row = driven_ref[pl.ds(t, 1), :]
        new_states = []
        outs = []
        for i in range(subs):
            d = d_row[:, i * lanes : (i + 1) * lanes]
            u = u_row[:, i * lanes : (i + 1) * lanes]
            state = jnp.exp(rates[i] * d) * states[i] + u * b_rows
            new_states.append(state)
            outs.append(jnp.sum(c_rows * state, axis=0, keepdims=True))
        y_ref[pl.ds(t, 1), :] = jnp.concatenate(outs, axis=1)
        return tuple(new_states)

    first = tuple(start_ref[:, i * lanes : (i + 1) * lanes] for i in range(subs))
    lax.fori_loop(0, tokens_here, step, first, unroll=8)


def sweep(start_state, a_neg, delta, driven, b_in, c_out):
    tokens_here, channels = delta.shape
    nstate = b_in.shape[1]
    lanes = 128
    block = 512
    b_wide = jnp.broadcast_to(b_in[:, :, None], (tokens_here, nstate, lanes))
    c_wide = jnp.broadcast_to(c_out[:, :, None], (tokens_here, nstate, lanes))
    row_spec = pl.BlockSpec((tokens_here, block), lambda k: (0, k))
    state_spec = pl.BlockSpec((nstate, block), lambda k: (0, k))
    wide_spec = pl.BlockSpec((tokens_here, nstate, lanes), lambda k: (0, 0, 0))
    return pl.pallas_call(
        sweep_kernel,
        out_shape=jax.ShapeDtypeStruct((tokens_here, channels), jnp.float32),
        grid=(channels // block,),
        in_specs=[row_spec, row_spec, state_spec, state_spec, wide_spec, wide_spec],
        out_specs=row_spec,
        cost_estimate=pl.CostEstimate(
            flops=8 * tokens_here * nstate * channels,
            transcendentals=tokens_here * nstate * channels,
            bytes_accessed=4 * (3 * tokens_here * channels + 2 * nstate * channels),
        ),
    )(delta, driven, a_neg, start_state, b_wide, c_wide)


def per_device(
    x_act, dt_low, b_c, w_dt, dt_bias, a_log, d_skip, w_router, expert_ids, w_up, w_down
):
    tokens_here = x_act.shape[1]
    channels = x_act.shape[2]
    nstate = a_log.shape[0]
    xfloat = x_act[0].astype(jnp.float32)
    pre = jnp.dot(dt_low[0], w_dt, preferred_element_type=jnp.float32)
    delta = jax.nn.softplus(pre + dt_bias)
    a_neg = -jnp.exp(a_log)
    driven = delta * xfloat
    b_in = b_c[0, :, :nstate]
    c_out = b_c[0, :, nstate:]
    cumulated = jnp.cumsum(delta, axis=0)
    pieces = max(1, channels // 512)
    span = channels // pieces
    ends = []
    for lower in range(0, channels, span):
        exponent = a_neg[None, :, lower : lower + span] * (
            cumulated[-1, lower : lower + span][None, None, :]
            - cumulated[:, None, lower : lower + span]
        )
        ends.append(
            jnp.sum(
                jnp.exp(exponent) * driven[:, None, lower : lower + span] * b_in[:, :, None], axis=0
            )
        )
    local = sweep(jnp.zeros_like(a_neg), a_neg, delta, driven, b_in, c_out)
    start = carry_in(a_neg, cumulated[-1], jnp.concatenate(ends, axis=1))
    start, local, w_up, w_down = lax.optimization_barrier((start, local, w_up, w_down))
    carried = []
    for lower in range(0, channels, span):
        decay = jnp.exp(a_neg[None, :, lower : lower + span] * cumulated[:, None, lower : lower + span])
        carried.append(
            jnp.sum(decay * start[None, :, lower : lower + span] * c_out[:, :, None], axis=1)
        )
    scanned = local + jnp.concatenate(carried, axis=1)
    mixer = (scanned + d_skip * xfloat).astype(jnp.bfloat16)
    experts_count = w_router.shape[0]
    owners = lax.axis_size("exp")
    capacity = 5 * tokens_here // owners
    picks = expert_ids[0]
    logits = jnp.dot(mixer, w_router.T, preferred_element_type=jnp.float32)
    chosen = jnp.take_along_axis(logits, picks, axis=1)
    first = jax.nn.sigmoid(chosen[:, 0] - chosen[:, 1])
    second = 1.0 - first
    flat_ids = picks.reshape(-1)
    onehot = (flat_ids[:, None] == jnp.arange(experts_count, dtype=jnp.int32)[None, :]).astype(
        jnp.int32
    )
    position = (jnp.sum(onehot * jnp.cumsum(onehot, axis=0), axis=1) - 1).reshape(tokens_here, 2)
    halves = owners // experts_count
    dest = jnp.arange(owners, dtype=jnp.int32)[:, None, None] // halves
    slot = jnp.arange(capacity, dtype=jnp.int32)[None, :, None]
    hit = [
        (dest == picks[None, None, :, c]) & (slot == position[None, None, :, c]) for c in range(2)
    ]
    dispatch = (hit[0] | hit[1]).astype(jnp.bfloat16)
    outgoing = jnp.einsum(
        "jst,tc->jsc", dispatch, mixer, preferred_element_type=jnp.float32
    ).astype(jnp.bfloat16)
    incoming = lax.all_to_all(outgoing, "exp", split_axis=0, concat_axis=0, tiled=True)
    pre_hidden = jnp.einsum(
        "jsc,ch->jsh",
        incoming,
        lax.all_gather(w_up, "seq", axis=1, tiled=True)[0],
        preferred_element_type=jnp.float32,
    )
    hidden = jax.nn.silu(pre_hidden).astype(jnp.bfloat16)
    partial_out = lax.optimization_barrier(
        jnp.einsum(
            "jsh,hc->jsc",
            hidden,
            lax.all_gather(w_down, "seq", axis=2, tiled=True)[0],
            preferred_element_type=jnp.float32,
        ).astype(jnp.bfloat16)
    )
    returned = lax.all_to_all(partial_out, "exp", split_axis=0, concat_axis=0, tiled=True)
    gather = jnp.stack(hit).astype(jnp.bfloat16)
    picked = jnp.einsum(
        "kjst,jsc->ktc", gather, returned, preferred_element_type=jnp.float32
    ).astype(jnp.bfloat16).astype(jnp.float32)
    routed = first[:, None] * picked[0] + second[:, None] * picked[1]
    return (mixer.astype(jnp.float32) + routed).astype(jnp.bfloat16)[None]


def solution(mesh):
    in_specs = (
        P("exp", "seq", None),
        P("exp", "seq", None),
        P("exp", "seq", None),
        P(),
        P(),
        P(),
        P(),
        P(),
        P("exp", "seq", None),
        P("exp", "seq", None),
        P("exp", None, "seq"),
    )
    out_specs = P("exp", "seq", None)
    return jax.shard_map(
        per_device, mesh=mesh, in_specs=in_specs, out_specs=out_specs, check_vma=False
    )
```

```python
import jax
import jax.numpy as jnp
from jax import lax
from jax.experimental import pallas as pl
from jax.sharding import PartitionSpec as P


def from_behind(value, axis, by):
    count = lax.axis_size(axis)
    pairs = [(i, i + by) for i in range(count) if 0 <= i + by < count]
    return lax.ppermute(value, axis, pairs)


def carry_in(a_neg, total_delta, end_state):
    count = lax.axis_size("seq")
    me = lax.axis_index("seq")
    high = total_delta.astype(jnp.bfloat16)
    low = (total_delta - high.astype(jnp.float32)).astype(jnp.bfloat16)
    packed = jnp.concatenate([high[None], low[None], end_state.astype(jnp.bfloat16)], axis=0)
    every = lax.all_gather(packed, "seq").astype(jnp.float32)
    state = jnp.zeros_like(end_state)
    for k in range(count - 1):
        total = every[k, 0] + every[k, 1]
        folded = jnp.exp(a_neg * total[None, :]) * state + every[k, 2:]
        state = jnp.where(k < me, folded, state)
    return state


def sweep_kernel(delta_ref, driven_ref, a_ref, start_ref, b_ref, c_ref, y_ref):
    tokens_here = delta_ref.shape[0]
    lanes = b_ref.shape[2]
    subs = delta_ref.shape[1] // lanes
    rates = [a_ref[:, i * lanes : (i + 1) * lanes] for i in range(subs)]

    def step(t, states):
        b_rows = b_ref[t]
        c_rows = c_ref[t]
        d_row = delta_ref[pl.ds(t, 1), :]
        u_row = driven_ref[pl.ds(t, 1), :]
        new_states = []
        outs = []
        for i in range(subs):
            d = d_row[:, i * lanes : (i + 1) * lanes]
            u = u_row[:, i * lanes : (i + 1) * lanes]
            state = jnp.exp(rates[i] * d) * states[i] + u * b_rows
            new_states.append(state)
            outs.append(jnp.sum(c_rows * state, axis=0, keepdims=True))
        y_ref[pl.ds(t, 1), :] = jnp.concatenate(outs, axis=1)
        return tuple(new_states)

    first = tuple(start_ref[:, i * lanes : (i + 1) * lanes] for i in range(subs))
    lax.fori_loop(0, tokens_here, step, first, unroll=8)


def sweep(start_state, a_neg, delta, driven, b_in, c_out):
    tokens_here, channels = delta.shape
    nstate = b_in.shape[1]
    lanes = 128
    block = 512
    b_wide = jnp.broadcast_to(b_in[:, :, None], (tokens_here, nstate, lanes))
    c_wide = jnp.broadcast_to(c_out[:, :, None], (tokens_here, nstate, lanes))
    row_spec = pl.BlockSpec((tokens_here, block), lambda k: (0, k))
    state_spec = pl.BlockSpec((nstate, block), lambda k: (0, k))
    wide_spec = pl.BlockSpec((tokens_here, nstate, lanes), lambda k: (0, 0, 0))
    return pl.pallas_call(
        sweep_kernel,
        out_shape=jax.ShapeDtypeStruct((tokens_here, channels), jnp.float32),
        grid=(channels // block,),
        in_specs=[row_spec, row_spec, state_spec, state_spec, wide_spec, wide_spec],
        out_specs=row_spec,
        cost_estimate=pl.CostEstimate(
            flops=8 * tokens_here * nstate * channels,
            transcendentals=tokens_here * nstate * channels,
            bytes_accessed=4 * (3 * tokens_here * channels + 2 * nstate * channels),
        ),
    )(delta, driven, a_neg, start_state, b_wide, c_wide)


def per_device(
    x_act, dt_low, b_c, w_dt, dt_bias, a_log, d_skip, w_router, expert_ids, w_up, w_down
):
    tokens_here = x_act.shape[1]
    channels = x_act.shape[2]
    nstate = a_log.shape[0]
    xfloat = x_act[0].astype(jnp.float32)
    pre = jnp.dot(dt_low[0], w_dt, preferred_element_type=jnp.float32)
    delta = jax.nn.softplus(pre + dt_bias)
    a_neg = -jnp.exp(a_log)
    driven = delta * xfloat
    b_in = b_c[0, :, :nstate]
    c_out = b_c[0, :, nstate:]
    cumulated = jnp.cumsum(delta, axis=0)
    pieces = max(1, channels // 512)
    span = channels // pieces
    ends = []
    for lower in range(0, channels, span):
        exponent = a_neg[None, :, lower : lower + span] * (
            cumulated[-1, lower : lower + span][None, None, :]
            - cumulated[:, None, lower : lower + span]
        )
        ends.append(
            jnp.sum(
                jnp.exp(exponent) * driven[:, None, lower : lower + span] * b_in[:, :, None], axis=0
            )
        )
    local = sweep(jnp.zeros_like(a_neg), a_neg, delta, driven, b_in, c_out)
    start = carry_in(a_neg, cumulated[-1], jnp.concatenate(ends, axis=1))
    start, local, w_up, w_down = lax.optimization_barrier((start, local, w_up, w_down))
    carried = []
    for lower in range(0, channels, span):
        decay = jnp.exp(a_neg[None, :, lower : lower + span] * cumulated[:, None, lower : lower + span])
        carried.append(
            jnp.sum(decay * start[None, :, lower : lower + span] * c_out[:, :, None], axis=1)
        )
    scanned = local + jnp.concatenate(carried, axis=1)
    mixer = (scanned + d_skip * xfloat).astype(jnp.bfloat16)
    experts_count = w_router.shape[0]
    owners = lax.axis_size("exp")
    capacity = 5 * tokens_here // owners
    picks = expert_ids[0]
    logits = jnp.dot(mixer, w_router.T, preferred_element_type=jnp.float32)
    chosen = jnp.take_along_axis(logits, picks, axis=1)
    first = jax.nn.sigmoid(chosen[:, 0] - chosen[:, 1])
    second = 1.0 - first
    flat_ids = picks.reshape(-1)
    onehot = (flat_ids[:, None] == jnp.arange(experts_count, dtype=jnp.int32)[None, :]).astype(
        jnp.int32
    )
    position = (jnp.sum(onehot * jnp.cumsum(onehot, axis=0), axis=1) - 1).reshape(tokens_here, 2)
    halves = owners // experts_count
    dest = jnp.arange(owners, dtype=jnp.int32)[:, None, None] // halves
    slot = jnp.arange(capacity, dtype=jnp.int32)[None, :, None]
    hit = [
        (dest == picks[None, None, :, c]) & (slot == position[None, None, :, c]) for c in range(2)
    ]
    dispatch = (hit[0] | hit[1]).astype(jnp.bfloat16)
    outgoing = jnp.einsum(
        "jst,tc->jsc", dispatch, mixer, preferred_element_type=jnp.float32
    ).astype(jnp.bfloat16)
    incoming = lax.all_to_all(outgoing, "exp", split_axis=0, concat_axis=0, tiled=True)
    pre_hidden = jnp.einsum(
        "jsc,ch->jsh",
        incoming,
        lax.all_gather(w_up, "seq", axis=1, tiled=True)[0],
        preferred_element_type=jnp.float32,
    )
    hidden = jax.nn.silu(pre_hidden).astype(jnp.bfloat16)
    partial_out = lax.optimization_barrier(
        jnp.einsum(
            "jsh,hc->jsc",
            hidden,
            lax.all_gather(w_down, "seq", axis=2, tiled=True)[0],
            preferred_element_type=jnp.float32,
        ).astype(jnp.bfloat16)
    )
    returned = lax.all_to_all(partial_out, "exp", split_axis=0, concat_axis=0, tiled=True)
    gather = jnp.stack(hit).astype(jnp.bfloat16)
    picked = jnp.einsum(
        "kjst,jsc->ktc", gather, returned, preferred_element_type=jnp.float32
    ).astype(jnp.bfloat16).astype(jnp.float32)
    routed = first[:, None] * picked[0] + second[:, None] * picked[1]
    return (mixer.astype(jnp.float32) + routed).astype(jnp.bfloat16)[None]


def solution(mesh):
    in_specs = (
        P("exp", "seq", None),
        P("exp", "seq", None),
        P("exp", "seq", None),
        P(),
        P(),
        P(),
        P(),
        P(),
        P("exp", "seq", None),
        P("exp", "seq", None),
        P("exp", None, "seq"),
    )
    out_specs = P("exp", "seq", None)
    return jax.shard_map(
        per_device, mesh=mesh, in_specs=in_specs, out_specs=out_specs, check_vma=False
    )
```

```python
import jax
import jax.numpy as jnp
from jax import lax
from jax.experimental import pallas as pl
from jax.sharding import PartitionSpec as P


def from_behind(value, axis, by):
    count = lax.axis_size(axis)
    pairs = [(i, i + by) for i in range(count) if 0 <= i + by < count]
    return lax.ppermute(value, axis, pairs)


def carry_in(a_neg, total_delta, end_state):
    count = lax.axis_size("seq")
    me = lax.axis_index("seq")
    high = total_delta.astype(jnp.bfloat16)
    low = (total_delta - high.astype(jnp.float32)).astype(jnp.bfloat16)
    packed = jnp.concatenate([high[None], low[None], end_state.astype(jnp.bfloat16)], axis=0)
    every = lax.all_gather(packed, "seq").astype(jnp.float32)

    def fold(k, state):
        packet = every[k]
        folded = jnp.exp(a_neg * (packet[0] + packet[1])[None, :]) * state + packet[2:]
        return jnp.where(k < me, folded, state)

    return lax.fori_loop(0, count - 1, fold, jnp.zeros_like(end_state))


def sweep_kernel(delta_ref, driven_ref, a_ref, start_ref, b_ref, c_ref, y_ref):
    tokens_here = delta_ref.shape[0]
    lanes = b_ref.shape[2]
    subs = delta_ref.shape[1] // lanes
    rates = [a_ref[:, i * lanes : (i + 1) * lanes] for i in range(subs)]

    def step(t, states):
        b_rows = b_ref[t]
        c_rows = c_ref[t]
        d_row = delta_ref[pl.ds(t, 1), :]
        u_row = driven_ref[pl.ds(t, 1), :]
        new_states = []
        outs = []
        for i in range(subs):
            d = d_row[:, i * lanes : (i + 1) * lanes]
            u = u_row[:, i * lanes : (i + 1) * lanes]
            state = jnp.exp(rates[i] * d) * states[i] + u * b_rows
            new_states.append(state)
            outs.append(jnp.sum(c_rows * state, axis=0, keepdims=True))
        y_ref[pl.ds(t, 1), :] = jnp.concatenate(outs, axis=1)
        return tuple(new_states)

    first = tuple(start_ref[:, i * lanes : (i + 1) * lanes] for i in range(subs))
    lax.fori_loop(0, tokens_here, step, first, unroll=8)


def sweep(start_state, a_neg, delta, driven, b_in, c_out):
    tokens_here, channels = delta.shape
    nstate = b_in.shape[1]
    lanes = 128
    block = 512
    b_wide = jnp.broadcast_to(b_in[:, :, None], (tokens_here, nstate, lanes))
    c_wide = jnp.broadcast_to(c_out[:, :, None], (tokens_here, nstate, lanes))
    row_spec = pl.BlockSpec((tokens_here, block), lambda k: (0, k))
    state_spec = pl.BlockSpec((nstate, block), lambda k: (0, k))
    wide_spec = pl.BlockSpec((tokens_here, nstate, lanes), lambda k: (0, 0, 0))
    return pl.pallas_call(
        sweep_kernel,
        out_shape=jax.ShapeDtypeStruct((tokens_here, channels), jnp.float32),
        grid=(channels // block,),
        in_specs=[row_spec, row_spec, state_spec, state_spec, wide_spec, wide_spec],
        out_specs=row_spec,
        cost_estimate=pl.CostEstimate(
            flops=8 * tokens_here * nstate * channels,
            transcendentals=tokens_here * nstate * channels,
            bytes_accessed=4 * (3 * tokens_here * channels + 2 * nstate * channels),
        ),
    )(delta, driven, a_neg, start_state, b_wide, c_wide)


def per_device(
    x_act, dt_low, b_c, w_dt, dt_bias, a_log, d_skip, w_router, expert_ids, w_up, w_down
):
    tokens_here = x_act.shape[1]
    channels = x_act.shape[2]
    nstate = a_log.shape[0]
    xfloat = x_act[0].astype(jnp.float32)
    pre = jnp.dot(dt_low[0], w_dt, preferred_element_type=jnp.float32)
    delta = jax.nn.softplus(pre + dt_bias)
    a_neg = -jnp.exp(a_log)
    driven = delta * xfloat
    b_in = b_c[0, :, :nstate]
    c_out = b_c[0, :, nstate:]
    cumulated = jnp.cumsum(delta, axis=0)
    pieces = max(1, channels // 2048)
    span = channels // pieces
    ends = []
    for lower in range(0, channels, span):
        exponent = a_neg[None, :, lower : lower + span] * (
            cumulated[-1, lower : lower + span][None, None, :]
            - cumulated[:, None, lower : lower + span]
        )
        ends.append(
            jnp.sum(
                jnp.exp(exponent) * driven[:, None, lower : lower + span] * b_in[:, :, None], axis=0
            )
        )
    local = sweep(jnp.zeros_like(a_neg), a_neg, delta, driven, b_in, c_out)
    start = carry_in(a_neg, cumulated[-1], jnp.concatenate(ends, axis=1))
    start, local, w_up, w_down = lax.optimization_barrier((start, local, w_up, w_down))
    carried = []
    for lower in range(0, channels, span):
        decay = jnp.exp(a_neg[None, :, lower : lower + span] * cumulated[:, None, lower : lower + span])
        carried.append(
            jnp.sum(decay * start[None, :, lower : lower + span] * c_out[:, :, None], axis=1)
        )
    scanned = local + jnp.concatenate(carried, axis=1)
    mixer = (scanned + d_skip * xfloat).astype(jnp.bfloat16)
    experts_count = w_router.shape[0]
    owners = lax.axis_size("exp")
    capacity = 5 * tokens_here // owners
    picks = expert_ids[0]
    logits = jnp.dot(mixer, w_router.T, preferred_element_type=jnp.float32)
    chosen = jnp.take_along_axis(logits, picks, axis=1)
    first = jax.nn.sigmoid(chosen[:, 0] - chosen[:, 1])
    second = 1.0 - first
    flat_ids = picks.reshape(-1)
    onehot = (flat_ids[:, None] == jnp.arange(experts_count, dtype=jnp.int32)[None, :]).astype(
        jnp.int32
    )
    position = (jnp.sum(onehot * jnp.cumsum(onehot, axis=0), axis=1) - 1).reshape(tokens_here, 2)
    halves = owners // experts_count
    dest = jnp.arange(owners, dtype=jnp.int32)[:, None, None] // halves
    slot = jnp.arange(capacity, dtype=jnp.int32)[None, :, None]
    hit = [
        (dest == picks[None, None, :, c]) & (slot == position[None, None, :, c]) for c in range(2)
    ]
    dispatch = (hit[0] | hit[1]).astype(jnp.bfloat16)
    outgoing = jnp.einsum(
        "jst,tc->jsc", dispatch, mixer, preferred_element_type=jnp.float32
    ).astype(jnp.bfloat16)
    incoming = lax.all_to_all(outgoing, "exp", split_axis=0, concat_axis=0, tiled=True)
    pre_hidden = jnp.einsum(
        "jsc,ch->jsh",
        incoming,
        lax.all_gather(w_up, "seq", axis=1, tiled=True)[0],
        preferred_element_type=jnp.float32,
    )
    hidden = jax.nn.silu(pre_hidden).astype(jnp.bfloat16)
    partial_out = lax.optimization_barrier(
        jnp.einsum(
            "jsh,hc->jsc",
            hidden,
            lax.all_gather(w_down, "seq", axis=2, tiled=True)[0],
            preferred_element_type=jnp.float32,
        ).astype(jnp.bfloat16)
    )
    returned = lax.all_to_all(partial_out, "exp", split_axis=0, concat_axis=0, tiled=True)
    gather = jnp.stack(hit).astype(jnp.bfloat16)
    picked = jnp.einsum(
        "kjst,jsc->ktc", gather, returned, preferred_element_type=jnp.float32
    ).astype(jnp.bfloat16).astype(jnp.float32)
    routed = first[:, None] * picked[0] + second[:, None] * picked[1]
    return (mixer.astype(jnp.float32) + routed).astype(jnp.bfloat16)[None]


def solution(mesh):
    in_specs = (
        P("exp", "seq", None),
        P("exp", "seq", None),
        P("exp", "seq", None),
        P(),
        P(),
        P(),
        P(),
        P(),
        P("exp", "seq", None),
        P("exp", "seq", None),
        P("exp", None, "seq"),
    )
    out_specs = P("exp", "seq", None)
    return jax.shard_map(
        per_device, mesh=mesh, in_specs=in_specs, out_specs=out_specs, check_vma=False
    )
```

```python
import jax
import jax.numpy as jnp
from jax import lax
from jax.experimental import pallas as pl
from jax.sharding import PartitionSpec as P


def from_behind(value, axis, by):
    count = lax.axis_size(axis)
    pairs = [(i, i + by) for i in range(count) if 0 <= i + by < count]
    return lax.ppermute(value, axis, pairs)


def carry_in(a_neg, total_delta, end_state):
    count = lax.axis_size("seq")
    me = lax.axis_index("seq")
    high = total_delta.astype(jnp.bfloat16)
    low = (total_delta - high.astype(jnp.float32)).astype(jnp.bfloat16)
    packed = jnp.concatenate([high[None], low[None], end_state.astype(jnp.bfloat16)], axis=0)
    every = lax.all_gather(packed, "seq").astype(jnp.float32)
    state = jnp.zeros_like(end_state)
    for k in range(count - 1):
        total = every[k, 0] + every[k, 1]
        folded = jnp.exp(a_neg * total[None, :]) * state + every[k, 2:]
        state = jnp.where(k < me, folded, state)
    return state


def sweep_kernel(delta_ref, driven_ref, a_ref, start_ref, b_ref, c_ref, y_ref):
    tokens_here = delta_ref.shape[0]
    lanes = b_ref.shape[2]
    subs = delta_ref.shape[1] // lanes
    rates = [a_ref[:, i * lanes : (i + 1) * lanes] for i in range(subs)]

    def step(t, states):
        b_rows = b_ref[t]
        c_rows = c_ref[t]
        d_row = delta_ref[pl.ds(t, 1), :]
        u_row = driven_ref[pl.ds(t, 1), :]
        new_states = []
        outs = []
        for i in range(subs):
            d = d_row[:, i * lanes : (i + 1) * lanes]
            u = u_row[:, i * lanes : (i + 1) * lanes]
            state = jnp.exp(rates[i] * d) * states[i] + u * b_rows
            new_states.append(state)
            outs.append(jnp.sum(c_rows * state, axis=0, keepdims=True))
        y_ref[pl.ds(t, 1), :] = jnp.concatenate(outs, axis=1)
        return tuple(new_states)

    first = tuple(start_ref[:, i * lanes : (i + 1) * lanes] for i in range(subs))
    lax.fori_loop(0, tokens_here, step, first, unroll=8)


def sweep(start_state, a_neg, delta, driven, b_in, c_out):
    tokens_here, channels = delta.shape
    nstate = b_in.shape[1]
    lanes = 128
    block = 512
    b_wide = jnp.broadcast_to(b_in[:, :, None], (tokens_here, nstate, lanes))
    c_wide = jnp.broadcast_to(c_out[:, :, None], (tokens_here, nstate, lanes))
    row_spec = pl.BlockSpec((tokens_here, block), lambda k: (0, k))
    state_spec = pl.BlockSpec((nstate, block), lambda k: (0, k))
    wide_spec = pl.BlockSpec((tokens_here, nstate, lanes), lambda k: (0, 0, 0))
    return pl.pallas_call(
        sweep_kernel,
        out_shape=jax.ShapeDtypeStruct((tokens_here, channels), jnp.float32),
        grid=(channels // block,),
        in_specs=[row_spec, row_spec, state_spec, state_spec, wide_spec, wide_spec],
        out_specs=row_spec,
        cost_estimate=pl.CostEstimate(
            flops=8 * tokens_here * nstate * channels,
            transcendentals=tokens_here * nstate * channels,
            bytes_accessed=4 * (3 * tokens_here * channels + 2 * nstate * channels),
        ),
    )(delta, driven, a_neg, start_state, b_wide, c_wide)


def per_device(
    x_act, dt_low, b_c, w_dt, dt_bias, a_log, d_skip, w_router, expert_ids, w_up, w_down
):
    tokens_here = x_act.shape[1]
    channels = x_act.shape[2]
    nstate = a_log.shape[0]
    xfloat = x_act[0].astype(jnp.float32)
    pre = jnp.dot(dt_low[0], w_dt, preferred_element_type=jnp.float32)
    delta = jax.nn.softplus(pre + dt_bias)
    a_neg = -jnp.exp(a_log)
    driven = delta * xfloat
    b_in = b_c[0, :, :nstate]
    c_out = b_c[0, :, nstate:]
    cumulated = jnp.cumsum(delta, axis=0)
    pieces = max(1, channels // 512)
    span = channels // pieces
    ends = []
    for lower in range(0, channels, span):
        exponent = a_neg[None, :, lower : lower + span] * (
            cumulated[-1, lower : lower + span][None, None, :]
            - cumulated[:, None, lower : lower + span]
        )
        ends.append(
            jnp.sum(
                jnp.exp(exponent) * driven[:, None, lower : lower + span] * b_in[:, :, None], axis=0
            )
        )
    local = sweep(jnp.zeros_like(a_neg), a_neg, delta, driven, b_in, c_out)
    start = carry_in(a_neg, cumulated[-1], jnp.concatenate(ends, axis=1))
    start, local, w_up, w_down = lax.optimization_barrier((start, local, w_up, w_down))
    carried = []
    for lower in range(0, channels, span):
        decay = jnp.exp(a_neg[:, None, lower : lower + span] * cumulated[None, :, lower : lower + span])
        carried.append(
            jnp.sum(decay * start[:, None, lower : lower + span] * c_out.T[:, :, None], axis=0)
        )
    scanned = local + jnp.concatenate(carried, axis=1)
    mixer = (scanned + d_skip * xfloat).astype(jnp.bfloat16)
    experts_count = w_router.shape[0]
    owners = lax.axis_size("exp")
    capacity = 5 * tokens_here // owners
    picks = expert_ids[0]
    logits = jnp.dot(mixer, w_router.T, preferred_element_type=jnp.float32)
    chosen = jnp.take_along_axis(logits, picks, axis=1)
    first = jax.nn.sigmoid(chosen[:, 0] - chosen[:, 1])
    second = 1.0 - first
    flat_ids = picks.reshape(-1)
    onehot = (flat_ids[:, None] == jnp.arange(experts_count, dtype=jnp.int32)[None, :]).astype(
        jnp.int32
    )
    position = (jnp.sum(onehot * jnp.cumsum(onehot, axis=0), axis=1) - 1).reshape(tokens_here, 2)
    halves = owners // experts_count
    dest = jnp.arange(owners, dtype=jnp.int32)[:, None, None] // halves
    slot = jnp.arange(capacity, dtype=jnp.int32)[None, :, None]
    hit = [
        (dest == picks[None, None, :, c]) & (slot == position[None, None, :, c]) for c in range(2)
    ]
    dispatch = (hit[0] | hit[1]).astype(jnp.bfloat16)
    outgoing = jnp.einsum(
        "jst,tc->jsc", dispatch, mixer, preferred_element_type=jnp.float32
    ).astype(jnp.bfloat16)
    incoming = lax.all_to_all(outgoing, "exp", split_axis=0, concat_axis=0, tiled=True)
    pre_hidden = jnp.einsum(
        "jsc,ch->jsh",
        incoming,
        lax.all_gather(w_up, "seq", axis=1, tiled=True)[0],
        preferred_element_type=jnp.float32,
    )
    hidden = jax.nn.silu(pre_hidden).astype(jnp.bfloat16)
    partial_out = lax.optimization_barrier(
        jnp.einsum(
            "jsh,hc->jsc",
            hidden,
            lax.all_gather(w_down, "seq", axis=2, tiled=True)[0],
            preferred_element_type=jnp.float32,
        ).astype(jnp.bfloat16)
    )
    returned = lax.all_to_all(partial_out, "exp", split_axis=0, concat_axis=0, tiled=True)
    gather = jnp.stack(hit).astype(jnp.bfloat16)
    picked = jnp.einsum(
        "kjst,jsc->ktc", gather, returned, preferred_element_type=jnp.float32
    ).astype(jnp.bfloat16).astype(jnp.float32)
    routed = first[:, None] * picked[0] + second[:, None] * picked[1]
    return (mixer.astype(jnp.float32) + routed).astype(jnp.bfloat16)[None]


def solution(mesh):
    in_specs = (
        P("exp", "seq", None),
        P("exp", "seq", None),
        P("exp", "seq", None),
        P(),
        P(),
        P(),
        P(),
        P(),
        P("exp", "seq", None),
        P("exp", "seq", None),
        P("exp", None, "seq"),
    )
    out_specs = P("exp", "seq", None)
    return jax.shard_map(
        per_device, mesh=mesh, in_specs=in_specs, out_specs=out_specs, check_vma=False
    )
```

```python
import jax
import jax.numpy as jnp
from jax import lax
from jax.experimental import pallas as pl
from jax.sharding import PartitionSpec as P


def from_behind(value, axis, by):
    count = lax.axis_size(axis)
    pairs = [(i, i + by) for i in range(count) if 0 <= i + by < count]
    return lax.ppermute(value, axis, pairs)


def carry_in(a_neg, total_delta, end_state):
    count = lax.axis_size("seq")
    me = lax.axis_index("seq")
    high = total_delta.astype(jnp.bfloat16)
    low = (total_delta - high.astype(jnp.float32)).astype(jnp.bfloat16)
    packed = jnp.concatenate([high[None], low[None], end_state.astype(jnp.bfloat16)], axis=0)
    every = lax.all_gather(packed, "seq").astype(jnp.float32)
    state = jnp.zeros_like(end_state)
    for k in range(count - 1):
        total = every[k, 0] + every[k, 1]
        folded = jnp.exp(a_neg * total[None, :]) * state + every[k, 2:]
        state = jnp.where(k < me, folded, state)
    return state


def sweep_kernel(delta_ref, driven_ref, a_ref, start_ref, b_ref, c_ref, y_ref):
    tokens_here = delta_ref.shape[0]
    lanes = b_ref.shape[2]
    subs = delta_ref.shape[1] // lanes
    rates = [a_ref[:, i * lanes : (i + 1) * lanes] for i in range(subs)]

    def step(t, states):
        b_rows = b_ref[t]
        c_rows = c_ref[t]
        d_row = delta_ref[pl.ds(t, 1), :]
        u_row = driven_ref[pl.ds(t, 1), :]
        new_states = []
        outs = []
        for i in range(subs):
            d = d_row[:, i * lanes : (i + 1) * lanes]
            u = u_row[:, i * lanes : (i + 1) * lanes]
            state = jnp.exp(rates[i] * d) * states[i] + u * b_rows
            new_states.append(state)
            outs.append(jnp.sum(c_rows * state, axis=0, keepdims=True))
        y_ref[pl.ds(t, 1), :] = jnp.concatenate(outs, axis=1)
        return tuple(new_states)

    first = tuple(start_ref[:, i * lanes : (i + 1) * lanes] for i in range(subs))
    lax.fori_loop(0, tokens_here, step, first, unroll=8)


def sweep(start_state, a_neg, delta, driven, b_in, c_out):
    tokens_here, channels = delta.shape
    nstate = b_in.shape[1]
    lanes = 128
    block = 512
    b_wide = jnp.broadcast_to(b_in[:, :, None], (tokens_here, nstate, lanes))
    c_wide = jnp.broadcast_to(c_out[:, :, None], (tokens_here, nstate, lanes))
    row_spec = pl.BlockSpec((tokens_here, block), lambda k: (0, k))
    state_spec = pl.BlockSpec((nstate, block), lambda k: (0, k))
    wide_spec = pl.BlockSpec((tokens_here, nstate, lanes), lambda k: (0, 0, 0))
    return pl.pallas_call(
        sweep_kernel,
        out_shape=jax.ShapeDtypeStruct((tokens_here, channels), jnp.float32),
        grid=(channels // block,),
        in_specs=[row_spec, row_spec, state_spec, state_spec, wide_spec, wide_spec],
        out_specs=row_spec,
        cost_estimate=pl.CostEstimate(
            flops=8 * tokens_here * nstate * channels,
            transcendentals=tokens_here * nstate * channels,
            bytes_accessed=4 * (3 * tokens_here * channels + 2 * nstate * channels),
        ),
    )(delta, driven, a_neg, start_state, b_wide, c_wide)


def per_device(
    x_act, dt_low, b_c, w_dt, dt_bias, a_log, d_skip, w_router, expert_ids, w_up, w_down
):
    tokens_here = x_act.shape[1]
    channels = x_act.shape[2]
    nstate = a_log.shape[0]
    xfloat = x_act[0].astype(jnp.float32)
    pre = jnp.dot(dt_low[0], w_dt, preferred_element_type=jnp.float32)
    delta = jax.nn.softplus(pre + dt_bias)
    a_neg = -jnp.exp(a_log)
    driven = delta * xfloat
    b_in = b_c[0, :, :nstate]
    c_out = b_c[0, :, nstate:]
    order = jnp.arange(tokens_here, dtype=jnp.int32)
    lower_ones = (order[:, None] >= order[None, :]).astype(jnp.float32)
    cumulated = jnp.dot(lower_ones, delta, precision=lax.Precision.HIGHEST)
    pieces = max(1, channels // 512)
    span = channels // pieces
    ends = []
    for lower in range(0, channels, span):
        exponent = a_neg[None, :, lower : lower + span] * (
            cumulated[-1, lower : lower + span][None, None, :]
            - cumulated[:, None, lower : lower + span]
        )
        ends.append(
            jnp.sum(
                jnp.exp(exponent) * driven[:, None, lower : lower + span] * b_in[:, :, None], axis=0
            )
        )
    local = sweep(jnp.zeros_like(a_neg), a_neg, delta, driven, b_in, c_out)
    start = carry_in(a_neg, cumulated[-1], jnp.concatenate(ends, axis=1))
    start, local, w_up, w_down = lax.optimization_barrier((start, local, w_up, w_down))
    carried = []
    for lower in range(0, channels, span):
        decay = jnp.exp(a_neg[:, None, lower : lower + span] * cumulated[None, :, lower : lower + span])
        carried.append(
            jnp.sum(decay * start[:, None, lower : lower + span] * c_out.T[:, :, None], axis=0)
        )
    scanned = local + jnp.concatenate(carried, axis=1)
    mixer = (scanned + d_skip * xfloat).astype(jnp.bfloat16)
    experts_count = w_router.shape[0]
    owners = lax.axis_size("exp")
    capacity = 5 * tokens_here // owners
    picks = expert_ids[0]
    logits = jnp.dot(mixer, w_router.T, preferred_element_type=jnp.float32)
    chosen = jnp.take_along_axis(logits, picks, axis=1)
    first = jax.nn.sigmoid(chosen[:, 0] - chosen[:, 1])
    second = 1.0 - first
    flat_ids = picks.reshape(-1)
    onehot = (flat_ids[:, None] == jnp.arange(experts_count, dtype=jnp.int32)[None, :]).astype(
        jnp.int32
    )
    position = (jnp.sum(onehot * jnp.cumsum(onehot, axis=0), axis=1) - 1).reshape(tokens_here, 2)
    halves = owners // experts_count
    dest = jnp.arange(owners, dtype=jnp.int32)[:, None, None] // halves
    slot = jnp.arange(capacity, dtype=jnp.int32)[None, :, None]
    hit = [
        (dest == picks[None, None, :, c]) & (slot == position[None, None, :, c]) for c in range(2)
    ]
    dispatch = (hit[0] | hit[1]).astype(jnp.bfloat16)
    outgoing = jnp.einsum(
        "jst,tc->jsc", dispatch, mixer, preferred_element_type=jnp.float32
    ).astype(jnp.bfloat16)
    incoming = lax.all_to_all(outgoing, "exp", split_axis=0, concat_axis=0, tiled=True)
    pre_hidden = jnp.einsum(
        "jsc,ch->jsh",
        incoming,
        lax.all_gather(w_up, "seq", axis=1, tiled=True)[0],
        preferred_element_type=jnp.float32,
    )
    hidden = jax.nn.silu(pre_hidden).astype(jnp.bfloat16)
    partial_out = lax.optimization_barrier(
        jnp.einsum(
            "jsh,hc->jsc",
            hidden,
            lax.all_gather(w_down, "seq", axis=2, tiled=True)[0],
            preferred_element_type=jnp.float32,
        ).astype(jnp.bfloat16)
    )
    returned = lax.all_to_all(partial_out, "exp", split_axis=0, concat_axis=0, tiled=True)
    gather = jnp.stack(hit).astype(jnp.bfloat16)
    picked = jnp.einsum(
        "kjst,jsc->ktc", gather, returned, preferred_element_type=jnp.float32
    ).astype(jnp.bfloat16).astype(jnp.float32)
    routed = first[:, None] * picked[0] + second[:, None] * picked[1]
    return (mixer.astype(jnp.float32) + routed).astype(jnp.bfloat16)[None]


def solution(mesh):
    in_specs = (
        P("exp", "seq", None),
        P("exp", "seq", None),
        P("exp", "seq", None),
        P(),
        P(),
        P(),
        P(),
        P(),
        P("exp", "seq", None),
        P("exp", "seq", None),
        P("exp", None, "seq"),
    )
    out_specs = P("exp", "seq", None)
    return jax.shard_map(
        per_device, mesh=mesh, in_specs=in_specs, out_specs=out_specs, check_vma=False
    )
```
